256 devices in a mesh: tok: 64 (over z, x, core), wt: 4 (over y).
Axes of the slice: x: 4, y: 4, z: 8, core: 2. Of those that a mesh axis runs over, the one named last changes fastest.
Arguments:
- hidden_in: bfloat16 [15360, 5120], P('tok', 'wt'), may hold values from -6 to 6
- qkv_weight: bfloat16 [5120, 3584], P('tok', 'wt'), may hold values from -0.078125 to 0.078125
- qkv_bias: bfloat16 [3584], P('wt'), may hold values from -30 to 30
- page_pool: bfloat16 [192, 128, 1024], P('tok', None, 'wt'), may hold values from -36 to 36
- page_table: int32 [3, 50], replicated, may hold values from 0 to 191, as said below
- cached_lengths: int32 [3], replicated, may hold values from 1 to 1280
- token_request: int32 [15360], replicated, may hold values from 0 to 2, as said below
- token_position: int32 [15360], P('tok'), may hold values from 1 to 6399, as said below
Outputs:
- attended: bfloat16 [15360, 2560], P('tok', 'wt')
- new_pool: bfloat16 [192, 128, 1024], P('tok', None, 'wt')
The draws below stay inside these ranges and needn't reach their ends.
Inputs may be any that keep to these rules, and one draw needn't show every extreme that they name: `page_table`: entries are distinct slots of the pool; the owner of slot g along tok is g div 3. `token_request`: new tokens come in 3 blocks of 5120, one request a block, in the order drawn. `token_position`: A request's new tokens have the consecutive positions cached_lengths[r] to cached_lengths[r] + 5119, in order.
All inputs are finite; a program needn't handle non-finite values.
Results may differ from the reference program's by a relative error of at most 0.0035.
The reference program's roundings to bfloat16 on the way count: a program that leaves them out, or rounds other values in their place, can miss the bound.
Values may be sent and summed in bfloat16 or wider, within the bound.
No kernel may reach another device: no remote copies, remote signals or barrier semaphores. Data moves between devices by JAX's collectives and lax.ppermute only.
A program may use at most 128 MiB of HBM per device.

```python
import math
import jax
import jax.numpy as jnp
from jax import lax

D = 5120
HEADS = 20
KVH = 4
HD = 128
PAGE = 128
REQS = 3
TOK_DEV = 240
GROUP = 5
QKVW = 3584
TOKENS = 15360
NEW = 5120
CMAX = 1280
CPAGES = 10
MAXPAGES = 50
SLOTS = 3
POOL = 192


def request_layout(key):
    lengths = jax.random.randint(jax.random.fold_in(key, 11), (REQS,), 1, CMAX + 1)
    longest = jax.random.randint(jax.random.fold_in(key, 12), (), 0, REQS)
    lengths = jnp.where(jnp.arange(REQS) == longest, CMAX, lengths).astype(jnp.int32)
    order = jax.random.permutation(jax.random.fold_in(key, 13), REQS).astype(jnp.int32)
    return (lengths, order)


def draw_cached_lengths(key, part):
    lengths, order = request_layout(key)
    return lengths


def draw_token_request(key, part):
    lengths, order = request_layout(key)
    return order[jnp.arange(TOKENS) // NEW].astype(jnp.int32)


def draw_token_position(key, part):
    lengths, order = request_layout(key)
    owner = order[jnp.arange(TOKENS) // NEW]
    return (lengths[owner] + jnp.arange(TOKENS) % NEW).astype(jnp.int32)


def draw_page_table(key, part):
    lengths, order = request_layout(key)
    slot_ids = jnp.arange(POOL, dtype=jnp.int32)
    special_slot = TOKENS // TOK_DEV // 2 * SLOTS
    ranking = jax.random.permutation(jax.random.fold_in(key, 21), POOL).astype(jnp.int32)
    ranking = jnp.where(slot_ids == 0, -3, ranking)
    ranking = jnp.where(slot_ids == POOL - 1, -2, ranking)
    ranking = jnp.where(slot_ids == special_slot, -4, ranking)
    chosen = jnp.argsort(ranking, stable=True)[:REQS * MAXPAGES].astype(jnp.int32)
    mixing = jax.random.permutation(jax.random.fold_in(key, 22), REQS * MAXPAGES)
    flat = chosen[mixing].astype(jnp.int32)
    entry_ids = jnp.arange(REQS * MAXPAGES, dtype=jnp.int32)
    target = (order[0] * MAXPAGES + lengths[order[0]] // PAGE).astype(jnp.int32)
    holder = jnp.sum(jnp.where(flat == special_slot, entry_ids, 0)).astype(jnp.int32)
    displaced = jnp.sum(jnp.where(entry_ids == target, flat, 0)).astype(jnp.int32)
    flat = jnp.where(entry_ids == target, special_slot, jnp.where(entry_ids == holder, displaced, flat))
    return flat.reshape(REQS, MAXPAGES).astype(jnp.int32)


def hot_layout(key):
    half = HD // 2
    reach = math.sqrt(math.sqrt(HD))
    key_top = 8.0 * reach
    query_top = 7.8 * reach
    sign_table = jnp.where(jax.random.bernoulli(jax.random.fold_in(key, 41), 0.5, (KVH, 4)), 1.0, -1.0)
    key_strength = jnp.exp(jax.random.uniform(jax.random.fold_in(key, 42), (KVH,), minval=math.log(0.25 * key_top), maxval=math.log(key_top)))
    strong = jax.random.randint(jax.random.fold_in(key, 43), (), 0, KVH)
    head_ids = jnp.arange(KVH)
    key_strength = jnp.where(head_ids == strong, key_top, key_strength)
    query_strength = jnp.exp(jax.random.uniform(jax.random.fold_in(key, 44), (KVH, GROUP), minval=math.log(0.01 * query_top), maxval=math.log(query_top)))
    chosen = jax.random.randint(jax.random.fold_in(key, 45), (), 0, GROUP)
    query_strength = jnp.where((head_ids[:, None] == strong) & (jnp.arange(GROUP)[None, :] == chosen), query_top, query_strength)
    dim_ids = jnp.arange(HD)
    hot_marks = jnp.stack([dim_ids == half - 2, dim_ids == half - 1, dim_ids == HD - 2, dim_ids == HD - 1]).astype(jnp.float32)
    pattern = jnp.sum(sign_table[:, :, None] * hot_marks[None], 1)
    return (pattern, key_strength, query_strength)


def draw_qkv_bias(key, part):
    pattern, key_strength, query_strength = hot_layout(key)
    base_noise = jnp.clip(0.5 * jax.random.normal(jax.random.fold_in(key, 46), (KVH, GROUP + 2, HD)), -3.0, 3.0)
    strength = jnp.concatenate([query_strength, key_strength[:, None], jnp.zeros((KVH, 1), jnp.float32)], 1)
    hot_values = strength[:, :, None] * pattern[:, None, :]
    hot_mask = (jnp.abs(pattern)[:, None, :] > 0.5) & (strength[:, :, None] > 0.0)
    bias = jnp.where(hot_mask, hot_values, base_noise)
    return bias.reshape(QKVW).astype(jnp.bfloat16)


def draw_page_pool(key, part):
    pattern, key_strength, query_strength = hot_layout(key)
    pool_shape = (POOL, PAGE, KVH, 2 * HD)
    noise_part = jnp.clip(jax.random.normal(jax.random.fold_in(key, 47), pool_shape), -6.0, 6.0)
    key_lift = jnp.concatenate([key_strength[:, None] * pattern, jnp.zeros((KVH, HD), jnp.float32)], 1)
    return (noise_part + key_lift[None, None]).reshape(POOL, PAGE, 2 * KVH * HD).astype(jnp.bfloat16)


def shard_levels(stream_key, shape, shards, least, top_value):
    factor_of = 1.0
    for axis_at, shards_of in shards:
        draws = jax.random.uniform(jax.random.fold_in(jax.random.fold_in(stream_key, 6), axis_at), (shards_of,), jnp.float32, least / len(shards), top_value / len(shards))
        factor_of = factor_of * jnp.repeat(jnp.exp(draws), shape[axis_at] // shards_of).reshape((-1,) + (1,) * (len(shape) - 1 - axis_at))
    return factor_of


def gaussian(rng, extent, width, most, shards=(), kind=jnp.bfloat16):
    factor_of = shard_levels(rng, extent, shards, -0.22, 0.18) if shards else 1.0
    values = jax.random.normal(rng, extent, jnp.float32) * width * factor_of
    return jnp.minimum(jnp.maximum(values, -most), most).astype(kind)


def setup_inputs(seed: int = 0) -> dict:
    splits = jax.random.split(jax.random.key(seed), 9)
    hidden_in = gaussian(splits[0], (TOKENS, D), 1.0, 6.0, ((0, 64), (1, 4)))
    qkv_weight = gaussian(splits[1], (D, QKVW), D ** -0.5, 0.078125, ((0, 64), (1, 4)))
    qkv_bias = draw_qkv_bias(jax.random.fold_in(splits[8], 71), 0)
    page_pool = draw_page_pool(jax.random.fold_in(splits[8], 71), 0)
    page_table = draw_page_table(jax.random.fold_in(splits[8], 71), 0)
    cached_lengths = draw_cached_lengths(jax.random.fold_in(splits[8], 71), 0)
    token_request = draw_token_request(jax.random.fold_in(splits[8], 71), 0)
    token_position = draw_token_position(jax.random.fold_in(splits[8], 71), 0)
    return dict(hidden_in=hidden_in, qkv_weight=qkv_weight, qkv_bias=qkv_bias, page_pool=page_pool, page_table=page_table, cached_lengths=cached_lengths, token_request=token_request, token_position=token_position)


ROPE_BASE = 1000000.0
NEG = -1e30


def rotate(part, positions):
    half = HD // 2
    freq = jnp.exp(jnp.arange(half, dtype=jnp.float32) * (-2.0 * math.log(ROPE_BASE) / HD))
    angle = positions.astype(jnp.float32)[:, None] * freq[None, :]
    cosine = jnp.cos(angle)[:, None, None, :]
    sine = jnp.sin(angle)[:, None, None, :]
    first = part[..., :half]
    second = part[..., half:]
    return jnp.concatenate([first * cosine - second * sine, second * cosine + first * sine], -1)


def finish(proj, positions):
    groups = proj.reshape(proj.shape[0], -1, HEADS // KVH + 2, HD)
    turned = rotate(groups[:, :, :-1], positions)
    queries = turned[:, :, :-1].astype(jnp.bfloat16)
    fresh = jnp.concatenate([turned[:, :, -1], groups[:, :, -1]], -1).astype(jnp.bfloat16)
    return queries, fresh


def reference(hidden_in, qkv_weight, qkv_bias, page_pool, page_table, cached_lengths, token_request, token_position):
    proj = jnp.dot(hidden_in, qkv_weight, preferred_element_type=jnp.float32) + qkv_bias.astype(jnp.float32)
    queries, fresh = finish(proj, token_position)
    layered = page_pool.reshape(POOL, PAGE, KVH, 2 * HD)
    slot_of = page_table[token_request, token_position // PAGE]
    new_pool = layered.at[slot_of, token_position % PAGE].set(fresh).reshape(POOL, PAGE, 2 * KVH * HD)
    cache_ids = jnp.arange(CPAGES * PAGE, dtype=jnp.int32)
    cached_flag = jnp.concatenate([jnp.ones((CPAGES * PAGE,), bool), jnp.zeros((NEW,), bool)])
    outputs = []
    for block_index in range(REQS):
        start_row = block_index * NEW
        request = token_request[start_row]
        cached_rows = layered[page_table[request][:CPAGES]].reshape(CPAGES * PAGE, KVH, 2 * HD)
        key_rows = jnp.concatenate([cached_rows, fresh[start_row:start_row + NEW]], 0)
        keys = key_rows[..., :HD].astype(jnp.float32)
        values = key_rows[..., HD:].astype(jnp.float32)
        key_pos = jnp.concatenate([cache_ids, token_position[start_row:start_row + NEW].astype(jnp.int32)])
        key_ok = jnp.concatenate([cache_ids < cached_lengths[request], jnp.ones((NEW,), bool)])
        query_rows = queries[start_row:start_row + NEW].reshape(8, NEW // 8, KVH, GROUP, HD)
        query_pos = token_position[start_row:start_row + NEW].astype(jnp.int32).reshape(8, NEW // 8)

        def one_block(inputs, keys=keys, values=values, key_pos=key_pos, key_ok=key_ok):
            q_block, pos_block = inputs
            visible = key_ok[None, :] & (cached_flag[None, :] | (key_pos[None, :] <= pos_block[:, None]))
            scores = jnp.einsum("tgqd,kgd->gqtk", q_block.astype(jnp.float32), keys) * (HD ** -0.5)
            top = jnp.max(jnp.where(visible[None, None], scores, NEG), -1)
            probs = jnp.where(visible[None, None], jnp.exp(scores - top[..., None]), 0.0)
            totals = jnp.sum(probs, -1)
            mixed = jnp.einsum("gqtk,kgd->gqtd", probs.astype(jnp.bfloat16).astype(jnp.float32), values) / totals[..., None]
            return mixed.transpose(2, 0, 1, 3).reshape(NEW // 8, HEADS * HD).astype(jnp.bfloat16)

        outputs.append(lax.map(one_block, (query_rows, query_pos)).reshape(NEW, HEADS * HD))
    return jnp.concatenate(outputs, 0), new_pool
```

```python
import math

import jax
import jax.numpy as jnp
from jax import lax
from jax.experimental import pallas as pl
from jax.experimental.pallas import tpu as pltpu
from jax.sharding import PartitionSpec as P

HEADS = 20
KVH = 4
HD = 128
PAGE = 128


ROPE_BASE = 1000000.0
NEG = -1e30


def rotate(part, positions):
    half = HD // 2
    freq = jnp.exp(jnp.arange(half, dtype=jnp.float32) * (-2.0 * math.log(ROPE_BASE) / HD))
    angle = positions.astype(jnp.float32)[:, None] * freq[None, :]
    cosine = jnp.cos(angle)[:, None, None, :]
    sine = jnp.sin(angle)[:, None, None, :]
    first = part[..., :half]
    second = part[..., half:]
    return jnp.concatenate([first * cosine - second * sine, second * cosine + first * sine], -1)


def finish(proj, positions):
    groups = proj.reshape(proj.shape[0], -1, HEADS // KVH + 2, HD)
    turned = rotate(groups[:, :, :-1], positions)
    queries = turned[:, :, :-1].astype(jnp.bfloat16)
    fresh = jnp.concatenate([turned[:, :, -1], groups[:, :, -1]], -1).astype(jnp.bfloat16)
    return (queries, fresh)

def flash_body(off_ref, flag_ref, q_ref, qpos_ref, qreq_ref, kv_ref, kpos_ref, kreq_ref,
               m_in, l_in, acc_in, m_out, l_out, acc_out):
    j = pl.program_id(0)

    @pl.when(j == 0)
    def _():
        m_out[...] = m_in[...]
        l_out[...] = l_in[...]
        acc_out[...] = acc_in[...]

    @pl.when(flag_ref[j] > 0)
    def _():
        kv = kv_ref[...]
        keys = kv[:, :HD]
        values = kv[:, HD:]
        scores = lax.dot_general(q_ref[...], keys, (((1,), (1,)), ((), ())),
                                 preferred_element_type=jnp.float32) * HD ** (-0.5)
        shown = (kreq_ref[...] == qreq_ref[...]) & (kpos_ref[...] <= qpos_ref[...])
        maxima = m_out[...]
        peak = jnp.maximum(maxima, jnp.max(jnp.where(shown, scores, NEG), axis=1, keepdims=True))
        probs = jnp.where(shown, jnp.exp(scores - peak), 0.0)
        fade = jnp.exp(maxima - peak)
        l_out[...] = l_out[...] * fade + jnp.sum(probs, axis=1, keepdims=True)
        acc_out[...] = acc_out[...] * fade + jnp.dot(
            probs.astype(jnp.bfloat16), values, preferred_element_type=jnp.float32)
        m_out[...] = peak


def flash_part(state, q, qpos, qreq, kv, kpos, kreq, first_block, flags, block):
    maxima, totals, summed = state
    rows = q.shape[0]
    nb = kv.shape[0] // block
    steps = flags.shape[0]

    def kv_map(j, off, fl):
        return (jnp.minimum(off[0] + j, nb - 1), 0)

    def k_map(j, off, fl):
        return (0, jnp.minimum(off[0] + j, nb - 1))

    def whole(j, off, fl):
        return (0, 0)

    grid_spec = pltpu.PrefetchScalarGridSpec(
        num_scalar_prefetch=2,
        grid=(steps,),
        in_specs=[
            pl.BlockSpec((rows, HD), whole),
            pl.BlockSpec((rows, 1), whole),
            pl.BlockSpec((rows, 1), whole),
            pl.BlockSpec((block, 2 * HD), kv_map),
            pl.BlockSpec((1, block), k_map),
            pl.BlockSpec((1, block), k_map),
            pl.BlockSpec((rows, 1), whole),
            pl.BlockSpec((rows, 1), whole),
            pl.BlockSpec((rows, HD), whole),
        ],
        out_specs=[
            pl.BlockSpec((rows, 1), whole),
            pl.BlockSpec((rows, 1), whole),
            pl.BlockSpec((rows, HD), whole),
        ],
    )
    return pl.pallas_call(
        flash_body,
        grid_spec=grid_spec,
        out_shape=[
            jax.ShapeDtypeStruct((rows, 1), jnp.float32),
            jax.ShapeDtypeStruct((rows, 1), jnp.float32),
            jax.ShapeDtypeStruct((rows, HD), jnp.float32),
        ],
        compiler_params=pltpu.CompilerParams(dimension_semantics=("arbitrary",)),
    )(first_block.reshape(1), flags, q, qpos, qreq, kv, kpos.reshape(1, -1), kreq.reshape(1, -1),
      maxima, totals, summed)


def per_device(
    hidden_in,
    qkv_weight,
    qkv_bias,
    page_pool,
    page_table,
    cached_lengths,
    token_request,
    token_position,
):
    wt_count = 4
    wt_index = lax.axis_index("wt")
    pieces = [hidden_in] + [
        lax.ppermute(hidden_in, "wt", [(i, (i + k) % wt_count) for i in range(wt_count)])
        for k in range(1, wt_count)
    ]
    order = (wt_index - jnp.arange(wt_count, dtype=jnp.int32)) % wt_count
    stacked = jnp.take(jnp.stack(pieces, 0), order, axis=0)
    full_rows = jnp.transpose(stacked, (1, 0, 2)).reshape(hidden_in.shape[0], -1)
    weight_all = lax.all_gather(qkv_weight, "tok", axis=0, tiled=True)
    proj = jnp.dot(full_rows, weight_all, preferred_element_type=jnp.float32)
    proj = proj + qkv_bias.astype(jnp.float32)
    queries, fresh = finish(proj, token_position)
    tok_dev = hidden_in.shape[0]
    local_groups = fresh.shape[1]
    kv_flat = fresh.reshape(tok_dev, local_groups * 2 * HD)
    total_tokens = token_request.shape[0]
    requests = cached_lengths.shape[0]
    new_len = total_tokens // requests
    cache_pages = (new_len // 4 + PAGE - 1) // PAGE
    pages_per = page_table.shape[1]
    slot_count = page_pool.shape[0]
    tok_index = lax.axis_index("tok")
    first_token = tok_index * tok_dev
    my_request = lax.dynamic_slice_in_dim(token_request, first_token, tok_dev)
    request_ids = jnp.arange(requests, dtype=jnp.int32)
    block_owner = token_request.reshape(requests, new_len)[:, 0]
    request_start = new_len * jnp.sum(
        (block_owner[None, :] == request_ids[:, None]) * request_ids[None, :], 1
    )
    token_ids = jnp.arange(total_tokens, dtype=jnp.int32)
    onehot = (token_request[:, None] == request_ids[None, :]).astype(jnp.int32)
    key_position = token_ids + jnp.sum(onehot * (cached_lengths - request_start)[None, :], 1)
    cache_slots = page_table[:, :cache_pages].reshape(requests * cache_pages)
    kv_all = lax.all_gather(kv_flat, "tok", axis=0, tiled=True)
    kv_all, pool_src = lax.optimization_barrier((kv_all, page_pool))
    row_floor = first_token // new_len * new_len
    row_span = min(total_tokens, new_len + tok_dev)
    heads_per = HEADS // KVH
    q_rows = jnp.transpose(queries, (1, 2, 0, 3)).reshape(local_groups * heads_per * tok_dev, HD)
    qpos_rows = jnp.tile(token_position, local_groups * heads_per).reshape(-1, 1)
    qreq_rows = jnp.tile(my_request, local_groups * heads_per).reshape(-1, 1)
    state = (
        jnp.full((q_rows.shape[0], 1), NEG, jnp.float32),
        jnp.zeros((q_rows.shape[0], 1), jnp.float32),
        jnp.zeros((q_rows.shape[0], HD), jnp.float32),
    )
    req_max = jnp.max(
        jnp.where(my_request[None, :] == request_ids[:, None], token_position[None, :], -1), axis=1
    )
    fresh_block = 512
    fresh_steps = -(-row_span // fresh_block)
    first_fresh = row_floor // fresh_block
    intended = (first_fresh + jnp.arange(fresh_steps, dtype=jnp.int32))[:, None] * fresh_block + jnp.arange(
        fresh_block, dtype=jnp.int32
    )[None, :]
    inside = intended < total_tokens
    rows_in = jnp.clip(intended, 0, total_tokens - 1)
    seen = inside & (
        jnp.take(key_position, rows_in) <= jnp.take(req_max, jnp.take(token_request, rows_in))
    )
    fresh_flags = jnp.any(seen, axis=1).astype(jnp.int32)
    state = flash_part(
        state, q_rows, qpos_rows, qreq_rows, kv_all, key_position, token_request,
        first_fresh.astype(jnp.int32), fresh_flags, fresh_block,
    )
    pool_all = lax.all_gather(pool_src, "tok", axis=0, tiled=True)
    cache_slots = page_table[:, :cache_pages].reshape(requests * cache_pages)
    picked_rows = jnp.take(pool_all, cache_slots, axis=0).reshape(requests * cache_pages * PAGE, -1)
    cache_ids = jnp.arange(requests * cache_pages * PAGE, dtype=jnp.int32)
    cache_req = cache_ids // (cache_pages * PAGE)
    cache_in = cache_ids % (cache_pages * PAGE)
    cache_pos = jnp.where(cache_in < jnp.take(cached_lengths, cache_req), cache_in, 1 << 30)
    cache_block = 5 * PAGE
    cache_steps = cache_ids.shape[0] // cache_block
    cache_flags = jnp.any(
        (cache_pos <= jnp.take(req_max, cache_req)).reshape(cache_steps, cache_block), axis=1
    ).astype(jnp.int32)
    state = flash_part(
        state, q_rows, qpos_rows, qreq_rows, picked_rows, cache_pos, cache_req,
        jnp.zeros((), jnp.int32), cache_flags, cache_block,
    )
    pool_now = page_pool
    write_row_count = kv_all.shape[0]
    page_ids = jnp.arange(pages_per, dtype=jnp.int32)
    row_ids = jnp.arange(PAGE, dtype=jnp.int32)
    for slot_index in range(slot_count):
        global_slot = tok_index * slot_count + slot_index
        match = (page_table == global_slot).astype(jnp.int32)
        used = jnp.sum(match) > 0
        request = jnp.sum(match * request_ids[:, None])
        page_index = jnp.sum(match * page_ids[None, :])
        cached_here = jnp.sum(jnp.where(request_ids == request, cached_lengths, 0))
        start_here = jnp.sum(jnp.where(request_ids == request, request_start, 0))
        positions = page_index * PAGE + row_ids
        target = start_here + positions - cached_here
        valid = (
            used
            & (positions >= cached_here)
            & (positions < cached_here + new_len)
            & (target >= 0)
            & (target < 0 + write_row_count)
        )
        source = jnp.take(kv_all, jnp.clip(target - 0, 0, write_row_count - 1), axis=0)
        pool_now = pool_now.at[slot_index].set(
            jnp.where(valid[:, None], source, pool_now[slot_index])
        )
    maxima, totals, summed = state
    attended = (
        (summed / totals)
        .reshape(local_groups, heads_per, tok_dev, HD)
        .transpose(2, 0, 1, 3)
        .reshape(tok_dev, local_groups * heads_per * HD)
        .astype(jnp.bfloat16)
    )
    return (attended, pool_now)


def solution(mesh):
    return jax.shard_map(
        per_device,
        mesh=mesh,
        in_specs=(
            P("tok", "wt"),
            P("tok", "wt"),
            P("wt"),
            P("tok", None, "wt"),
            P(),
            P(),
            P(),
            P("tok"),
        ),
        out_specs=(P("tok", "wt"), P("tok", None, "wt")),
        check_vma=False,
    )
```

```python
import math

import jax
import jax.numpy as jnp
from jax import lax
from jax.experimental import pallas as pl
from jax.experimental.pallas import tpu as pltpu
from jax.sharding import Mesh, PartitionSpec as P

HEADS = 20
KVH = 4
HD = 128
PAGE = 128


ROPE_BASE = 1000000.0
NEG = -1e30
TOK = ("z", "x", "c")


def ring(n, k):
    return [(i, (i + k) % n) for i in range(n)]


def shift_gather(piece, axis, n):
    idx = lax.axis_index(axis)
    parts = [piece] + [lax.ppermute(piece, axis, ring(n, k)) for k in range(1, n)]
    order = (idx - jnp.arange(n, dtype=jnp.int32)) % n
    return jnp.take(jnp.stack(parts, 0), order, axis=0)


def shift_reduce(chunks, axis, n):
    idx = lax.axis_index(axis)
    total = lax.dynamic_index_in_dim(chunks, idx, 0, keepdims=False)
    for k in range(1, n):
        piece = lax.dynamic_index_in_dim(chunks, (idx + k) % n, 0, keepdims=False)
        total = total + lax.ppermute(piece, axis, ring(n, k))
    return total


def sparse_allsum(contrib, zs, xs):
    rows = contrib.shape[0]
    half = rows // 2
    both = contrib + lax.ppermute(contrib, "c", ring(2, 1))
    mine = lax.dynamic_slice_in_dim(both, lax.axis_index("c") * half, half, 0)
    by_x = shift_reduce(mine.reshape(xs, half // xs, -1), "x", xs)
    by_z = shift_reduce(by_x.reshape(zs, half // xs // zs, -1), "z", zs)
    back_z = shift_gather(by_z, "z", zs).reshape(half // xs, -1)
    back_x = shift_gather(back_z, "x", xs).reshape(half, -1)
    return shift_gather(back_x, "c", 2).reshape(rows, -1)


def rotate(part, positions):
    half = HD // 2
    freq = jnp.exp(jnp.arange(half, dtype=jnp.float32) * (-2.0 * math.log(ROPE_BASE) / HD))
    angle = positions.astype(jnp.float32)[:, None] * freq[None, :]
    cosine = jnp.cos(angle)[:, None, None, :]
    sine = jnp.sin(angle)[:, None, None, :]
    first = part[..., :half]
    second = part[..., half:]
    return jnp.concatenate([first * cosine - second * sine, second * cosine + first * sine], -1)


def finish(proj, positions):
    groups = proj.reshape(proj.shape[0], -1, HEADS // KVH + 2, HD)
    turned = rotate(groups[:, :, :-1], positions)
    queries = turned[:, :, :-1].astype(jnp.bfloat16)
    fresh = jnp.concatenate([turned[:, :, -1], groups[:, :, -1]], -1).astype(jnp.bfloat16)
    return (queries, fresh)

def flash_body(off_ref, flag_ref, q_ref, qpos_ref, qreq_ref, kv_ref, kpos_ref, kreq_ref,
               m_in, l_in, acc_in, m_out, l_out, acc_out):
    j = pl.program_id(0)

    @pl.when(j == 0)
    def _():
        m_out[...] = m_in[...]
        l_out[...] = l_in[...]
        acc_out[...] = acc_in[...]

    @pl.when(flag_ref[j] > 0)
    def _():
        kv = kv_ref[...]
        keys = kv[:, :HD]
        values = kv[:, HD:]
        scores = lax.dot_general(q_ref[...], keys, (((1,), (1,)), ((), ())),
                                 preferred_element_type=jnp.float32) * HD ** (-0.5)
        shown = (kreq_ref[...] == qreq_ref[...]) & (kpos_ref[...] <= qpos_ref[...])
        maxima = m_out[...]
        peak = jnp.maximum(maxima, jnp.max(jnp.where(shown, scores, NEG), axis=1, keepdims=True))
        probs = jnp.where(shown, jnp.exp(scores - peak), 0.0)
        fade = jnp.exp(maxima - peak)
        l_out[...] = l_out[...] * fade + jnp.sum(probs, axis=1, keepdims=True)
        acc_out[...] = acc_out[...] * fade + jnp.dot(
            probs.astype(jnp.bfloat16), values, preferred_element_type=jnp.float32)
        m_out[...] = peak


def flash_part(state, q, qpos, qreq, kv, kpos, kreq, first_block, flags, block):
    maxima, totals, summed = state
    rows = q.shape[0]
    nb = kv.shape[0] // block
    steps = flags.shape[0]

    def kv_map(j, off, fl):
        return (jnp.minimum(off[0] + j, nb - 1), 0)

    def k_map(j, off, fl):
        return (0, jnp.minimum(off[0] + j, nb - 1))

    def whole(j, off, fl):
        return (0, 0)

    grid_spec = pltpu.PrefetchScalarGridSpec(
        num_scalar_prefetch=2,
        grid=(steps,),
        in_specs=[
            pl.BlockSpec((rows, HD), whole),
            pl.BlockSpec((rows, 1), whole),
            pl.BlockSpec((rows, 1), whole),
            pl.BlockSpec((block, 2 * HD), kv_map),
            pl.BlockSpec((1, block), k_map),
            pl.BlockSpec((1, block), k_map),
            pl.BlockSpec((rows, 1), whole),
            pl.BlockSpec((rows, 1), whole),
            pl.BlockSpec((rows, HD), whole),
        ],
        out_specs=[
            pl.BlockSpec((rows, 1), whole),
            pl.BlockSpec((rows, 1), whole),
            pl.BlockSpec((rows, HD), whole),
        ],
    )
    return pl.pallas_call(
        flash_body,
        grid_spec=grid_spec,
        out_shape=[
            jax.ShapeDtypeStruct((rows, 1), jnp.float32),
            jax.ShapeDtypeStruct((rows, 1), jnp.float32),
            jax.ShapeDtypeStruct((rows, HD), jnp.float32),
        ],
        compiler_params=pltpu.CompilerParams(dimension_semantics=("arbitrary",)),
    )(first_block.reshape(1), flags, q, qpos, qreq, kv, kpos.reshape(1, -1), kreq.reshape(1, -1),
      maxima, totals, summed)


def per_device(
    hidden_in,
    qkv_weight,
    qkv_bias,
    page_pool,
    page_table,
    cached_lengths,
    token_request,
    token_position,
):
    wt_count = 4
    wt_index = lax.axis_index("wt")
    pieces = [hidden_in] + [
        lax.ppermute(hidden_in, "wt", [(i, (i + k) % wt_count) for i in range(wt_count)])
        for k in range(1, wt_count)
    ]
    order = (wt_index - jnp.arange(wt_count, dtype=jnp.int32)) % wt_count
    stacked = jnp.take(jnp.stack(pieces, 0), order, axis=0)
    full_rows = jnp.transpose(stacked, (1, 0, 2)).reshape(hidden_in.shape[0], -1)
    weight_all = lax.all_gather(qkv_weight, TOK, axis=0, tiled=True)
    slot_count = page_pool.shape[0]
    cache_span = (token_request.shape[0] // cached_lengths.shape[0] // 4 + PAGE - 1) // PAGE
    cache_slots = page_table[:, :cache_span].reshape(-1)
    local_slot = cache_slots - lax.axis_index(TOK) * slot_count
    filled = jnp.zeros((cache_slots.shape[0],) + page_pool.shape[1:], page_pool.dtype)
    for slot_index in range(slot_count):
        filled = jnp.where((local_slot == slot_index)[:, None, None], page_pool[slot_index][None], filled)
    picked_all = sparse_allsum(filled.reshape(-1, filled.shape[-1]), 8, 4)
    weight_all, picked_all = lax.optimization_barrier((weight_all, picked_all))
    proj = jnp.dot(full_rows, weight_all, preferred_element_type=jnp.float32)
    proj = proj + qkv_bias.astype(jnp.float32)
    queries, fresh = finish(proj, token_position)
    tok_dev = hidden_in.shape[0]
    local_groups = fresh.shape[1]
    kv_flat = fresh.reshape(tok_dev, local_groups * 2 * HD)
    total_tokens = token_request.shape[0]
    requests = cached_lengths.shape[0]
    new_len = total_tokens // requests
    cache_pages = (new_len // 4 + PAGE - 1) // PAGE
    pages_per = page_table.shape[1]
    slot_count = page_pool.shape[0]
    tok_index = lax.axis_index(TOK)
    first_token = tok_index * tok_dev
    my_request = lax.dynamic_slice_in_dim(token_request, first_token, tok_dev)
    request_ids = jnp.arange(requests, dtype=jnp.int32)
    block_owner = token_request.reshape(requests, new_len)[:, 0]
    request_start = new_len * jnp.sum(
        (block_owner[None, :] == request_ids[:, None]) * request_ids[None, :], 1
    )
    token_ids = jnp.arange(total_tokens, dtype=jnp.int32)
    onehot = (token_request[:, None] == request_ids[None, :]).astype(jnp.int32)
    key_position = token_ids + jnp.sum(onehot * (cached_lengths - request_start)[None, :], 1)
    cache_slots = page_table[:, :cache_pages].reshape(requests * cache_pages)
    kv_all = lax.all_gather(kv_flat, TOK, axis=0, tiled=True)
    row_floor = first_token // new_len * new_len
    row_span = min(total_tokens, new_len + tok_dev)
    heads_per = HEADS // KVH
    q_rows = jnp.transpose(queries, (1, 2, 0, 3)).reshape(local_groups * heads_per * tok_dev, HD)
    qpos_rows = jnp.tile(token_position, local_groups * heads_per).reshape(-1, 1)
    qreq_rows = jnp.tile(my_request, local_groups * heads_per).reshape(-1, 1)
    state = (
        jnp.full((q_rows.shape[0], 1), NEG, jnp.float32),
        jnp.zeros((q_rows.shape[0], 1), jnp.float32),
        jnp.zeros((q_rows.shape[0], HD), jnp.float32),
    )
    req_max = jnp.max(
        jnp.where(my_request[None, :] == request_ids[:, None], token_position[None, :], -1), axis=1
    )
    fresh_block = 512
    fresh_steps = -(-row_span // fresh_block)
    first_fresh = row_floor // fresh_block
    window = fresh_steps * fresh_block
    pad_pos = jnp.concatenate([key_position, jnp.full((window,), 1 << 30, jnp.int32)])
    pad_req = jnp.concatenate([token_request, jnp.zeros((window,), jnp.int32)])
    win_pos = lax.dynamic_slice_in_dim(pad_pos, row_floor, window)
    win_req = lax.dynamic_slice_in_dim(pad_req, row_floor, window)
    win_top = jnp.full((window,), -1, jnp.int32)
    for request in range(requests):
        win_top = jnp.where(win_req == request, req_max[request], win_top)
    seen = (win_pos <= win_top).reshape(fresh_steps, fresh_block)
    fresh_flags = jnp.any(seen, axis=1).astype(jnp.int32)
    state = flash_part(
        state, q_rows, qpos_rows, qreq_rows, kv_all, key_position, token_request,
        first_fresh.astype(jnp.int32), fresh_flags, fresh_block,
    )
    state, kv_src = lax.optimization_barrier((state, kv_all))
    picked_rows = picked_all
    cache_in = jnp.arange(cache_pages * PAGE, dtype=jnp.int32)
    cache_pos = jnp.where(cache_in[None, :] < cached_lengths[:, None], cache_in[None, :], 1 << 30)
    cache_req = jnp.broadcast_to(request_ids[:, None], cache_pos.shape).reshape(-1)
    cache_block = 5 * PAGE
    cache_steps = cache_req.shape[0] // cache_block
    cache_flags = jnp.any(
        (cache_pos <= req_max[:, None]).reshape(cache_steps, cache_block), axis=1
    ).astype(jnp.int32)
    cache_pos = cache_pos.reshape(-1)
    state = flash_part(
        state, q_rows, qpos_rows, qreq_rows, picked_rows, cache_pos, cache_req,
        jnp.zeros((), jnp.int32), cache_flags, cache_block,
    )
    pool_now = page_pool
    write_row_count = kv_all.shape[0]
    page_ids = jnp.arange(pages_per, dtype=jnp.int32)
    row_ids = jnp.arange(PAGE, dtype=jnp.int32)
    for slot_index in range(slot_count):
        global_slot = tok_index * slot_count + slot_index
        match = (page_table == global_slot).astype(jnp.int32)
        used = jnp.sum(match) > 0
        request = jnp.sum(match * request_ids[:, None])
        page_index = jnp.sum(match * page_ids[None, :])
        cached_here = jnp.sum(jnp.where(request_ids == request, cached_lengths, 0))
        start_here = jnp.sum(jnp.where(request_ids == request, request_start, 0))
        positions = page_index * PAGE + row_ids
        target = start_here + positions - cached_here
        valid = (
            used
            & (positions >= cached_here)
            & (positions < cached_here + new_len)
            & (target >= 0)
            & (target < 0 + write_row_count)
        )
        first_row = start_here + page_index * PAGE - cached_here
        clamped = jnp.clip(first_row, 0, write_row_count - PAGE)
        shift = (first_row - clamped) % PAGE
        rows = lax.dynamic_slice_in_dim(kv_src, clamped, PAGE, 0)
        source = lax.dynamic_slice_in_dim(jnp.concatenate([rows, rows], 0), shift, PAGE, 0)
        pool_now = pool_now.at[slot_index].set(
            jnp.where(valid[:, None], source, pool_now[slot_index])
        )
    maxima, totals, summed = state
    attended = (
        (summed / totals)
        .reshape(local_groups, heads_per, tok_dev, HD)
        .transpose(2, 0, 1, 3)
        .reshape(tok_dev, local_groups * heads_per * HD)
        .astype(jnp.bfloat16)
    )
    return (attended, pool_now)


def solution(mesh):
    zs, xs = 8, 4
    sub = Mesh(mesh.devices.reshape(zs, xs, -1, mesh.devices.shape[1]), ("z", "x", "c", "wt"))
    return jax.shard_map(
        per_device,
        mesh=sub,
        in_specs=(
            P(TOK, "wt"),
            P(TOK, "wt"),
            P("wt"),
            P(TOK, None, "wt"),
            P(),
            P(),
            P(),
            P(TOK),
        ),
        out_specs=(P(TOK, "wt"), P(TOK, None, "wt")),
        check_vma=False,
    )
```

```python
import math

import jax
import jax.numpy as jnp
from jax import lax
from jax.experimental import pallas as pl
from jax.experimental.pallas import tpu as pltpu
from jax.sharding import Mesh, PartitionSpec as P

HEADS = 20
KVH = 4
HD = 128
PAGE = 128


ROPE_BASE = 1000000.0
NEG = -1e30
TOK = ("z", "x", "c")


def ring(n, k):
    return [(i, (i + k) % n) for i in range(n)]


def shift_gather(piece, axis, n):
    idx = lax.axis_index(axis)
    parts = [piece] + [lax.ppermute(piece, axis, ring(n, k)) for k in range(1, n)]
    order = (idx - jnp.arange(n, dtype=jnp.int32)) % n
    return jnp.take(jnp.stack(parts, 0), order, axis=0)


def shift_reduce(chunks, axis, n):
    idx = lax.axis_index(axis)
    total = lax.dynamic_index_in_dim(chunks, idx, 0, keepdims=False)
    for k in range(1, n):
        piece = lax.dynamic_index_in_dim(chunks, (idx + k) % n, 0, keepdims=False)
        total = total + lax.ppermute(piece, axis, ring(n, k))
    return total


def sparse_scatter(contrib, zs, xs):
    rows = contrib.shape[0]
    half = rows // 2
    both = contrib + lax.ppermute(contrib, "c", ring(2, 1))
    mine = lax.dynamic_slice_in_dim(both, lax.axis_index("c") * half, half, 0)
    by_x = shift_reduce(mine.reshape(xs, half // xs, -1), "x", xs)
    return shift_reduce(by_x.reshape(zs, half // xs // zs, -1), "z", zs)


def sparse_gather(by_z, rows, zs, xs):
    half = rows // 2
    back_z = shift_gather(by_z, "z", zs).reshape(half // xs, -1)
    back_x = shift_gather(back_z, "x", xs).reshape(half, -1)
    return shift_gather(back_x, "c", 2).reshape(rows, -1)


def rotate(part, positions):
    half = HD // 2
    freq = jnp.exp(jnp.arange(half, dtype=jnp.float32) * (-2.0 * math.log(ROPE_BASE) / HD))
    angle = positions.astype(jnp.float32)[:, None] * freq[None, :]
    cosine = jnp.cos(angle)[:, None, None, :]
    sine = jnp.sin(angle)[:, None, None, :]
    first = part[..., :half]
    second = part[..., half:]
    return jnp.concatenate([first * cosine - second * sine, second * cosine + first * sine], -1)


def finish(proj, positions):
    groups = proj.reshape(proj.shape[0], -1, HEADS // KVH + 2, HD)
    turned = rotate(groups[:, :, :-1], positions)
    queries = turned[:, :, :-1].astype(jnp.bfloat16)
    fresh = jnp.concatenate([turned[:, :, -1], groups[:, :, -1]], -1).astype(jnp.bfloat16)
    return (queries, fresh)

def flash_body(off_ref, flag_ref, q_ref, qpos_ref, qreq_ref, kv_ref, kpos_ref, kreq_ref,
               m_in, l_in, acc_in, m_out, l_out, acc_out):
    j = pl.program_id(0)

    @pl.when(j == 0)
    def _():
        m_out[...] = m_in[...]
        l_out[...] = l_in[...]
        acc_out[...] = acc_in[...]

    @pl.when(flag_ref[j] > 0)
    def _():
        kv = kv_ref[...]
        keys = kv[:, :HD]
        values = kv[:, HD:]
        scores = lax.dot_general(q_ref[...], keys, (((1,), (1,)), ((), ())),
                                 preferred_element_type=jnp.float32) * HD ** (-0.5)
        shown = (kreq_ref[...] == qreq_ref[...]) & (kpos_ref[...] <= qpos_ref[...])
        maxima = m_out[...]
        peak = jnp.maximum(maxima, jnp.max(jnp.where(shown, scores, NEG), axis=1, keepdims=True))
        probs = jnp.where(shown, jnp.exp(scores - peak), 0.0)
        fade = jnp.exp(maxima - peak)
        l_out[...] = l_out[...] * fade + jnp.sum(probs, axis=1, keepdims=True)
        acc_out[...] = acc_out[...] * fade + jnp.dot(
            probs.astype(jnp.bfloat16), values, preferred_element_type=jnp.float32)
        m_out[...] = peak


def flash_part(state, q, qpos, qreq, kv, kpos, kreq, first_block, flags, block):
    maxima, totals, summed = state
    rows = q.shape[0]
    nb = kv.shape[0] // block
    steps = flags.shape[0]

    def kv_map(j, off, fl):
        return (jnp.minimum(off[0] + j, nb - 1), 0)

    def k_map(j, off, fl):
        return (0, jnp.minimum(off[0] + j, nb - 1))

    def whole(j, off, fl):
        return (0, 0)

    grid_spec = pltpu.PrefetchScalarGridSpec(
        num_scalar_prefetch=2,
        grid=(steps,),
        in_specs=[
            pl.BlockSpec((rows, HD), whole),
            pl.BlockSpec((rows, 1), whole),
            pl.BlockSpec((rows, 1), whole),
            pl.BlockSpec((block, 2 * HD), kv_map),
            pl.BlockSpec((1, block), k_map),
            pl.BlockSpec((1, block), k_map),
            pl.BlockSpec((rows, 1), whole),
            pl.BlockSpec((rows, 1), whole),
            pl.BlockSpec((rows, HD), whole),
        ],
        out_specs=[
            pl.BlockSpec((rows, 1), whole),
            pl.BlockSpec((rows, 1), whole),
            pl.BlockSpec((rows, HD), whole),
        ],
    )
    return pl.pallas_call(
        flash_body,
        grid_spec=grid_spec,
        out_shape=[
            jax.ShapeDtypeStruct((rows, 1), jnp.float32),
            jax.ShapeDtypeStruct((rows, 1), jnp.float32),
            jax.ShapeDtypeStruct((rows, HD), jnp.float32),
        ],
        compiler_params=pltpu.CompilerParams(dimension_semantics=("arbitrary",)),
    )(first_block.reshape(1), flags, q, qpos, qreq, kv, kpos.reshape(1, -1), kreq.reshape(1, -1),
      maxima, totals, summed)


def per_device(
    hidden_in,
    qkv_weight,
    qkv_bias,
    page_pool,
    page_table,
    cached_lengths,
    token_request,
    token_position,
):
    wt_count = 4
    wt_index = lax.axis_index("wt")
    pieces = [hidden_in] + [
        lax.ppermute(hidden_in, "wt", [(i, (i + k) % wt_count) for i in range(wt_count)])
        for k in range(1, wt_count)
    ]
    order = (wt_index - jnp.arange(wt_count, dtype=jnp.int32)) % wt_count
    stacked = jnp.take(jnp.stack(pieces, 0), order, axis=0)
    full_rows = jnp.transpose(stacked, (1, 0, 2)).reshape(hidden_in.shape[0], -1)
    weight_all = lax.all_gather(qkv_weight, TOK, axis=0, tiled=True)
    slot_count = page_pool.shape[0]
    cache_span = (token_request.shape[0] // cached_lengths.shape[0] // 4 + PAGE - 1) // PAGE
    cache_slots = page_table[:, :cache_span].reshape(-1)
    local_slot = cache_slots - lax.axis_index(TOK) * slot_count
    filled = jnp.zeros((cache_slots.shape[0],) + page_pool.shape[1:], page_pool.dtype)
    for slot_index in range(slot_count):
        filled = jnp.where((local_slot == slot_index)[:, None, None], page_pool[slot_index][None], filled)
    picked_part = sparse_scatter(filled.reshape(-1, filled.shape[-1]), 8, 4)
    weight_all, picked_part = lax.optimization_barrier((weight_all, picked_part))
    picked_all = sparse_gather(picked_part, filled.shape[0] * filled.shape[1], 8, 4)
    proj = jnp.dot(full_rows, weight_all, preferred_element_type=jnp.float32)
    proj = proj + qkv_bias.astype(jnp.float32)
    queries, fresh = finish(proj, token_position)
    tok_dev = hidden_in.shape[0]
    local_groups = fresh.shape[1]
    kv_flat = fresh.reshape(tok_dev, local_groups * 2 * HD)
    total_tokens = token_request.shape[0]
    requests = cached_lengths.shape[0]
    new_len = total_tokens // requests
    cache_pages = (new_len // 4 + PAGE - 1) // PAGE
    pages_per = page_table.shape[1]
    slot_count = page_pool.shape[0]
    tok_index = lax.axis_index(TOK)
    first_token = tok_index * tok_dev
    my_request = lax.dynamic_slice_in_dim(token_request, first_token, tok_dev)
    request_ids = jnp.arange(requests, dtype=jnp.int32)
    block_owner = token_request.reshape(requests, new_len)[:, 0]
    request_start = new_len * jnp.sum(
        (block_owner[None, :] == request_ids[:, None]) * request_ids[None, :], 1
    )
    token_ids = jnp.arange(total_tokens, dtype=jnp.int32)
    onehot = (token_request[:, None] == request_ids[None, :]).astype(jnp.int32)
    key_position = token_ids + jnp.sum(onehot * (cached_lengths - request_start)[None, :], 1)
    cache_slots = page_table[:, :cache_pages].reshape(requests * cache_pages)
    kv_all = lax.all_gather(kv_flat, TOK, axis=0, tiled=True)
    row_floor = first_token // new_len * new_len
    row_span = min(total_tokens, new_len + tok_dev)
    heads_per = HEADS // KVH
    q_rows = jnp.transpose(queries, (1, 2, 0, 3)).reshape(local_groups * heads_per * tok_dev, HD)
    qpos_rows = jnp.tile(token_position, local_groups * heads_per).reshape(-1, 1)
    qreq_rows = jnp.tile(my_request, local_groups * heads_per).reshape(-1, 1)
    state = (
        jnp.full((q_rows.shape[0], 1), NEG, jnp.float32),
        jnp.zeros((q_rows.shape[0], 1), jnp.float32),
        jnp.zeros((q_rows.shape[0], HD), jnp.float32),
    )
    req_max = jnp.max(
        jnp.where(my_request[None, :] == request_ids[:, None], token_position[None, :], -1), axis=1
    )
    picked_rows = picked_all
    cache_in = jnp.arange(cache_pages * PAGE, dtype=jnp.int32)
    cache_pos = jnp.where(cache_in[None, :] < cached_lengths[:, None], cache_in[None, :], 1 << 30)
    cache_req = jnp.broadcast_to(request_ids[:, None], cache_pos.shape).reshape(-1)
    cache_block = 5 * PAGE
    cache_steps = cache_req.shape[0] // cache_block
    cache_flags = jnp.any(
        (cache_pos <= req_max[:, None]).reshape(cache_steps, cache_block), axis=1
    ).astype(jnp.int32)
    cache_pos = cache_pos.reshape(-1)
    state = flash_part(
        state, q_rows, qpos_rows, qreq_rows, picked_rows, cache_pos, cache_req,
        jnp.zeros((), jnp.int32), cache_flags, cache_block,
    )
    fresh_block = 512
    fresh_steps = -(-row_span // fresh_block)
    first_fresh = row_floor // fresh_block
    window = fresh_steps * fresh_block
    pad_pos = jnp.concatenate([key_position, jnp.full((window,), 1 << 30, jnp.int32)])
    pad_req = jnp.concatenate([token_request, jnp.zeros((window,), jnp.int32)])
    win_pos = lax.dynamic_slice_in_dim(pad_pos, row_floor, window)
    win_req = lax.dynamic_slice_in_dim(pad_req, row_floor, window)
    win_top = jnp.full((window,), -1, jnp.int32)
    for request in range(requests):
        win_top = jnp.where(win_req == request, req_max[request], win_top)
    seen = (win_pos <= win_top).reshape(fresh_steps, fresh_block)
    fresh_flags = jnp.any(seen, axis=1).astype(jnp.int32)
    state = flash_part(
        state, q_rows, qpos_rows, qreq_rows, kv_all, key_position, token_request,
        first_fresh.astype(jnp.int32), fresh_flags, fresh_block,
    )
    state, kv_src = lax.optimization_barrier((state, kv_all))
    pool_now = page_pool
    write_row_count = kv_all.shape[0]
    page_ids = jnp.arange(pages_per, dtype=jnp.int32)
    row_ids = jnp.arange(PAGE, dtype=jnp.int32)
    for slot_index in range(slot_count):
        global_slot = tok_index * slot_count + slot_index
        match = (page_table == global_slot).astype(jnp.int32)
        used = jnp.sum(match) > 0
        request = jnp.sum(match * request_ids[:, None])
        page_index = jnp.sum(match * page_ids[None, :])
        cached_here = jnp.sum(jnp.where(request_ids == request, cached_lengths, 0))
        start_here = jnp.sum(jnp.where(request_ids == request, request_start, 0))
        positions = page_index * PAGE + row_ids
        target = start_here + positions - cached_here
        valid = (
            used
            & (positions >= cached_here)
            & (positions < cached_here + new_len)
            & (target >= 0)
            & (target < 0 + write_row_count)
        )
        first_row = start_here + page_index * PAGE - cached_here
        clamped = jnp.clip(first_row, 0, write_row_count - PAGE)
        shift = (first_row - clamped) % PAGE
        rows = lax.dynamic_slice_in_dim(kv_src, clamped, PAGE, 0)
        source = lax.dynamic_slice_in_dim(jnp.concatenate([rows, rows], 0), shift, PAGE, 0)
        pool_now = pool_now.at[slot_index].set(
            jnp.where(valid[:, None], source, pool_now[slot_index])
        )
    maxima, totals, summed = state
    attended = (
        (summed / totals)
        .reshape(local_groups, heads_per, tok_dev, HD)
        .transpose(2, 0, 1, 3)
        .reshape(tok_dev, local_groups * heads_per * HD)
        .astype(jnp.bfloat16)
    )
    return (attended, pool_now)


def solution(mesh):
    zs, xs = 8, 4
    sub = Mesh(mesh.devices.reshape(zs, xs, -1, mesh.devices.shape[1]), ("z", "x", "c", "wt"))
    return jax.shard_map(
        per_device,
        mesh=sub,
        in_specs=(
            P(TOK, "wt"),
            P(TOK, "wt"),
            P("wt"),
            P(TOK, None, "wt"),
            P(),
            P(),
            P(),
            P(TOK),
        ),
        out_specs=(P(TOK, "wt"), P(TOK, None, "wt")),
        check_vma=False,
    )
```
